128 devices in a mesh: section: 4 (over z), expert: 32 (over y, x, core).
Axes of the slice: x: 4, y: 4, z: 4, core: 2. Of those that a mesh axis runs over, the one named last changes fastest.
Arguments:
- hidden_in: bfloat16 [4, 6144, 2048], P('section', 'expert'), may hold values from -6 to 6
- out_grad: bfloat16 [4, 6144, 2048], P('section', 'expert'), may hold values from -1.5 to 1.5
- routes: int32 [4, 6144, 2], P('section', 'expert'), may hold values from 0 to 31, all different within a row; in each aligned block of 192 rows (0 to 191, 192 to 383, ..., all dimensions but the last counted through in order) at most 24 rows name the same one
- mixing: bfloat16 [4, 6144, 2], P('section', 'expert'), may hold values from 0.099609375 to 0.8984375
- w_gate: bfloat16 [4, 32, 2048, 768], P('section', 'expert'), may hold values from -0.125 to 0.125
- w_up: bfloat16 [4, 32, 2048, 768], P('section', 'expert'), may hold values from -0.125 to 0.125
- w_down: bfloat16 [4, 32, 768, 2048], P('section', 'expert'), may hold values from -0.21875 to 0.21875
Outputs:
- grad_gate: bfloat16 [4, 32, 2048, 768], P('section', 'expert')
- grad_up: bfloat16 [4, 32, 2048, 768], P('section', 'expert')
- grad_down: bfloat16 [4, 32, 768, 2048], P('section', 'expert')
- handed: bfloat16 [4, 6144, 2048], P('section', 'expert')
- prob_grad: bfloat16 [4, 6144, 2], P('section', 'expert')
The draws below stay inside these ranges and needn't reach their ends.
Inputs may be any that keep to these rules, and one draw needn't show every extreme that they name: `routes`: the two experts of a token differ. Among the 192 tokens of one device (aligned blocks of the token dimension), no expert is named more than 24 times, and in some block some expert is named exactly 24 times; every expert is named by some token of each section.
All inputs are finite; a program needn't handle non-finite values.
Results may differ from the reference program's by a relative error of at most 0.012.
Values may be sent and summed in bfloat16 or wider, within the bound.
No kernel may reach another device: no remote copies, remote signals or barrier semaphores. Data moves between devices by JAX's collectives and lax.ppermute only.
A program may use at most 128 MiB of HBM per device.

```python
import math
import jax
import jax.numpy as jnp
import numpy as np
from jax import lax

D = 2048
FF = 768
TOK_DEV = 192
SECTIONS = 4
EXPERTS = 32
TOKENS = 6144
CAP = 24
N_EXPERT = 32


def level_of(rng, extent, pieces, smallest, high):
    factor_of, own = 1.0, jax.random.fold_in(rng, 6)
    for position, shards_of in pieces:
        draws = jnp.exp(jax.random.uniform(jax.random.fold_in(own, position), (shards_of,), jnp.float32, smallest / len(pieces), high / len(pieces)))
        factor_of = factor_of * jnp.repeat(draws, extent[position] // shards_of).reshape([-1 if axis == position else 1 for axis in range(len(extent))])
    return factor_of


def routed_block(rng, own, number, rows, amount, top, reach, slope):
    order = jax.random.permutation(rng, amount)
    crowded, ordinary = load_shares(amount, rows * top, reach, slope, True), load_shares(amount, rows * top, reach, slope, False)
    places = jnp.arange(amount)

    def named(lengths, offset_by):
        used = int((lengths > 0).sum())
        fixed = max(1, used // 4)
        moved = fixed + (places - fixed + offset_by * (used - fixed)) % max(1, amount - fixed)
        return jnp.zeros((amount,), jnp.int32).at[order[jnp.where(places < fixed, places, moved)]].set(jnp.asarray(lengths, jnp.int32))

    lengths = jnp.where(number % 4 == 0, named(crowded, number // 4), named(ordinary, number - number // 4 - 1))
    mixed = jax.random.permutation(jax.random.fold_in(own, 3), amount)
    donor, receiver = mixed[0:amount // 2 * 2:2], mixed[1:amount // 2 * 2:2]
    slack = jnp.minimum(lengths[donor] - 1, reach - lengths[receiver]) // 2
    slack = jnp.where((donor == order[0]) | (receiver == order[0]) | (lengths[receiver] == 0), 0, jnp.maximum(slack, 0))
    moved = jax.random.randint(jax.random.fold_in(own, 4), (amount // 2,), 0, 1 << 20) % (slack + 1)
    lengths = lengths.at[donor].add(-moved).at[receiver].add(moved)
    labels = jnp.searchsorted(jnp.cumsum(lengths), jnp.arange(rows * top), side="right").astype(jnp.int32)
    table = labels.reshape(top, rows).T
    table = table[jax.random.permutation(jax.random.fold_in(own, 1), rows)]
    offset_by = jax.random.randint(jax.random.fold_in(own, 2), (rows, 1), 0, top)
    return jnp.take_along_axis(table, (jnp.arange(top)[None, :] + offset_by) % top, axis=1)


def load_shares(number_of, total, limit, skew, full):
    loads = [(1 << 20) // math.isqrt(grade ** skew) + 1 for grade in range(1, number_of + 1)]
    largest = limit if full else min(limit, max(-(-total // number_of), total * loads[0] // sum(loads)))
    least = 1 if total - largest >= number_of - 1 else 0
    given, rest = [largest] + [least] * (number_of - 1), total - largest - least * (number_of - 1)
    while rest > 0:
        free = [i for i in range(1, number_of) if given[i] < largest] or [i for i in range(1, number_of) if given[i] < limit]
        mass, remaining = sum([loads[i] for i in free]), rest
        for i in free:
            extra = min(limit - given[i], max(1, remaining * loads[i] // mass), rest)
            given[i] = given[i] + extra
            rest = rest - extra
    return np.array(given)


def normal_values(rng, extent, deviation, bound, pieces=(), held_as=jnp.bfloat16):
    drawn = jax.random.normal(rng, extent, jnp.float32) * deviation
    if len(pieces) > 0:
        drawn = level_of(rng, extent, pieces, -0.22, 0.18) * drawn
    return jnp.clip(drawn, min=-bound, max=bound).astype(held_as)


def setup_inputs(seed: int = 0) -> dict:
    splits = jax.random.split(jax.random.key(seed), 8)
    hidden_in = normal_values(splits[0], (SECTIONS, TOKENS, D), 1.0, 6.0, ((0, 4), (1, 32)))
    out_grad = normal_values(splits[1], (SECTIONS, TOKENS, D), 0.25, 1.5, ((0, 4), (1, 32)))
    routes_keys = jax.random.split(jax.random.fold_in(splits[2], 1), SECTIONS * TOKENS // TOK_DEV)
    routes_turns = jax.random.permutation(jax.random.fold_in(splits[2], 3), SECTIONS * TOKENS // TOK_DEV)
    routes = jax.vmap(lambda own, number: routed_block(jax.random.fold_in(splits[2], 2), own, number, TOK_DEV, EXPERTS, 2, CAP, 2))(routes_keys, routes_turns).reshape((SECTIONS, TOKENS, 2))
    mixing = jnp.clip(0.099609375 + 0.7988281 * jax.random.uniform(splits[3], (SECTIONS, TOKENS, 2), jnp.float32) ** level_of(splits[3], (SECTIONS, TOKENS, 2), ((0, 4), (1, 32)), -0.2, 0.2), 0.099609375, 0.8984375).astype(jnp.bfloat16)
    w_gate = normal_values(splits[4], (SECTIONS, EXPERTS, D, FF), D ** -0.5, 0.125, ((0, 4), (1, 32)))
    w_up = normal_values(splits[5], (SECTIONS, EXPERTS, D, FF), D ** -0.5, 0.125, ((0, 4), (1, 32)))
    w_down = normal_values(splits[6], (SECTIONS, EXPERTS, FF, D), FF ** -0.5, 0.21875, ((0, 4), (1, 32)))
    return dict(hidden_in=hidden_in, out_grad=out_grad, routes=routes, mixing=mixing, w_gate=w_gate, w_up=w_up, w_down=w_down)


def expert_pass(rows_in, grad_rows, weight_rows, gate_mat, up_mat, down_mat):
    pre_gate = jnp.dot(rows_in, gate_mat, preferred_element_type=jnp.float32)
    pre_up = jnp.dot(rows_in, up_mat, preferred_element_type=jnp.float32)
    sigmoid_g = jax.nn.sigmoid(pre_gate)
    silu_g = pre_gate * sigmoid_g
    act_rows = (silu_g * pre_up).astype(jnp.bfloat16)
    expert_out = jnp.dot(act_rows, down_mat, preferred_element_type=jnp.float32).astype(jnp.bfloat16)
    prob_part = jnp.sum(grad_rows.astype(jnp.float32) * expert_out.astype(jnp.float32), axis=1).astype(jnp.bfloat16)
    scaled = (weight_rows.astype(jnp.float32)[:, None] * grad_rows.astype(jnp.float32)).astype(jnp.bfloat16)
    act_grad = jnp.dot(scaled, down_mat.T, preferred_element_type=jnp.float32)
    gate_pre = (act_grad * pre_up * sigmoid_g * (1.0 + pre_gate * (1.0 - sigmoid_g))).astype(jnp.bfloat16)
    up_pre = (act_grad * silu_g).astype(jnp.bfloat16)
    grad_down = jnp.dot(act_rows.T, scaled, preferred_element_type=jnp.float32).astype(jnp.bfloat16)
    grad_gate = jnp.dot(rows_in.T, gate_pre, preferred_element_type=jnp.float32).astype(jnp.bfloat16)
    grad_up = jnp.dot(rows_in.T, up_pre, preferred_element_type=jnp.float32).astype(jnp.bfloat16)
    in_grad = (jnp.dot(gate_pre, gate_mat.T, preferred_element_type=jnp.float32)
               + jnp.dot(up_pre, up_mat.T, preferred_element_type=jnp.float32)).astype(jnp.bfloat16)
    return grad_gate, grad_up, grad_down, in_grad, prob_part


def reference(hidden_in, out_grad, routes, mixing, w_gate, w_up, w_down):
    assign_rows = 2 * TOK_DEV
    expert_ids = jnp.arange(EXPERTS, dtype=jnp.int32)
    slot_count = N_EXPERT * CAP
    gate_list, up_list, down_list, input_list, prob_list = [], [], [], [], []
    for section_idx in range(SECTIONS):
        chosen = routes[section_idx].reshape(N_EXPERT, assign_rows).astype(jnp.int32)
        onehot = (chosen[:, :, None] == expert_ids[None, None, :]).astype(jnp.int32)
        slot_rank = jnp.sum(onehot * (jnp.cumsum(onehot, axis=1) - 1), axis=2)
        source = jnp.arange(N_EXPERT, dtype=jnp.int32)[:, None] * jnp.ones((1, assign_rows), jnp.int32)
        token_row = source * TOK_DEV + jnp.arange(assign_rows, dtype=jnp.int32)[None, :] // 2
        flat_slot = (chosen * slot_count + source * CAP + slot_rank).reshape(-1).astype(jnp.int32)
        slot_table = jnp.zeros((EXPERTS * slot_count,), jnp.int32).at[flat_slot].set(token_row.reshape(-1))
        weight_table = jnp.zeros((EXPERTS * slot_count,), jnp.bfloat16).at[flat_slot].set(mixing[section_idx].reshape(-1))
        rows_x = hidden_in[section_idx][slot_table].reshape(EXPERTS, slot_count, D)
        rows_g = out_grad[section_idx][slot_table].reshape(EXPERTS, slot_count, D)
        packed_in = (rows_x, rows_g, weight_table.reshape(EXPERTS, slot_count),
                     w_gate[section_idx], w_up[section_idx], w_down[section_idx])
        grad_gate, grad_up, grad_down, in_grad, prob_part = lax.map(lambda packed: expert_pass(*packed), packed_in)
        returned = in_grad.reshape(EXPERTS * slot_count, D)[flat_slot].reshape(TOKENS, 2, D)
        input_grad = (out_grad[section_idx].astype(jnp.float32)
                      + jnp.sum(returned.astype(jnp.float32), axis=1)).astype(jnp.bfloat16)
        prob_out = prob_part.reshape(-1)[flat_slot].reshape(TOKENS, 2)
        gate_list.append(grad_gate)
        up_list.append(grad_up)
        down_list.append(grad_down)
        input_list.append(input_grad)
        prob_list.append(prob_out)
    handed = jnp.stack(input_list[1:] + [jnp.zeros((TOKENS, D), jnp.bfloat16)])
    return (jnp.stack(gate_list), jnp.stack(up_list), jnp.stack(down_list), handed, jnp.stack(prob_list))
```

```python
import jax
import jax.numpy as jnp
from jax import lax
from jax.sharding import PartitionSpec as P


def shifted(block, axis, distance):
    devices = range(lax.axis_size(axis))
    route = [(i - distance, i) for i in devices if i - distance in devices]
    return lax.ppermute(block, axis, route)


def contract_rows(left, right):
    return lax.dot_general(
        left, right, (((0,), (0,)), ((), ())), preferred_element_type=jnp.float32
    )


def contract_cols(left, right):
    return lax.dot_general(
        left, right, (((1,), (1,)), ((), ())), preferred_element_type=jnp.float32
    )


def exchange(block, groups):
    lead = block.shape[0]
    parted = block.reshape((groups, lead // groups) + block.shape[1:])
    moved = lax.all_to_all(parted, "expert", split_axis=0, concat_axis=0, tiled=True)
    return moved.reshape(block.shape)


def per_device(hidden_in, out_grad, routes, mixing, w_gate, w_up, w_down):
    tokens_in = hidden_in[0]
    grads_in = out_grad[0]
    groups = lax.axis_size("expert")
    tok_rows = tokens_in.shape[0]
    capacity = 4 * tok_rows // groups
    slot_total = groups * capacity
    gate_mat = w_gate[0, 0]
    up_mat = w_up[0, 0]
    down_mat = w_down[0, 0]

    chosen = routes[0].reshape(-1)
    onehot = (chosen[:, None] == jnp.arange(groups, dtype=jnp.int32)[None, :]).astype(jnp.int32)
    slot_rank = jnp.sum(onehot * (jnp.cumsum(onehot, axis=0) - 1), axis=1)
    slot_index = (chosen * capacity + slot_rank).reshape(tok_rows, 2)
    slot_ids = jnp.arange(slot_total, dtype=jnp.int32)
    hit = slot_index[None, :, :] == slot_ids[:, None, None]
    pick = jnp.any(hit, axis=2).astype(jnp.bfloat16)
    slot_weight = jnp.sum(
        jnp.where(hit, mixing[0][None, :, :].astype(jnp.float32), 0.0), axis=(1, 2)
    ).astype(jnp.bfloat16)

    send_rows = jnp.dot(pick, tokens_in, preferred_element_type=jnp.float32).astype(jnp.bfloat16)
    send_grads = jnp.dot(pick, grads_in, preferred_element_type=jnp.float32).astype(jnp.bfloat16)

    rows_in = exchange(send_rows, groups)
    weight_in = exchange(slot_weight, groups)
    grad_rows = exchange(send_grads, groups)

    pre_gate = jnp.dot(rows_in, gate_mat, preferred_element_type=jnp.float32)
    pre_up = jnp.dot(rows_in, up_mat, preferred_element_type=jnp.float32)
    sigmoid_g = jax.nn.sigmoid(pre_gate)
    silu_g = pre_gate * sigmoid_g
    act_rows = (silu_g * pre_up).astype(jnp.bfloat16)
    expert_out = jnp.dot(act_rows, down_mat, preferred_element_type=jnp.float32).astype(
        jnp.bfloat16
    )
    prob_part = jnp.sum(
        grad_rows.astype(jnp.float32) * expert_out.astype(jnp.float32), axis=1
    ).astype(jnp.bfloat16)
    scaled = (weight_in.astype(jnp.float32)[:, None] * grad_rows.astype(jnp.float32)).astype(
        jnp.bfloat16
    )
    act_grad = contract_cols(scaled, down_mat)
    gate_pre = (act_grad * pre_up * sigmoid_g * (1.0 + pre_gate * (1.0 - sigmoid_g))).astype(
        jnp.bfloat16
    )
    up_pre = (act_grad * silu_g).astype(jnp.bfloat16)
    in_grad = (contract_cols(gate_pre, gate_mat) + contract_cols(up_pre, up_mat)).astype(
        jnp.bfloat16
    )

    back_grad = exchange(in_grad, groups)
    back_prob = exchange(prob_part, groups)

    grad_down = contract_rows(act_rows, scaled).astype(jnp.bfloat16)
    grad_gate = contract_rows(rows_in, gate_pre).astype(jnp.bfloat16)
    grad_up = contract_rows(rows_in, up_pre).astype(jnp.bfloat16)

    input_grad = (
        grads_in.astype(jnp.float32) + contract_rows(pick, back_grad)
    ).astype(jnp.bfloat16)
    prob_grad = jnp.sum(
        jnp.where(hit, back_prob.astype(jnp.float32)[:, None, None], 0.0), axis=0
    ).astype(jnp.bfloat16)
    handed = shifted(input_grad, "section", -1)
    return (
        grad_gate[None, None],
        grad_up[None, None],
        grad_down[None, None],
        handed[None],
        prob_grad[None],
    )


def solution(mesh):
    placed = (
        P("section", "expert", None),
        P("section", "expert", None),
        P("section", "expert", None),
        P("section", "expert", None),
        P("section", "expert", None, None),
        P("section", "expert", None, None),
        P("section", "expert", None, None),
    )
    return jax.shard_map(
        per_device,
        mesh=mesh,
        in_specs=placed,
        out_specs=(
            P("section", "expert", None, None),
            P("section", "expert", None, None),
            P("section", "expert", None, None),
            P("section", "expert", None),
            P("section", "expert", None),
        ),
        check_vma=False,
    )
```

```python
import jax
import jax.numpy as jnp
from jax import lax
from jax.sharding import PartitionSpec as P


def shifted(block, axis, distance):
    devices = range(lax.axis_size(axis))
    route = [(i - distance, i) for i in devices if i - distance in devices]
    return lax.ppermute(block, axis, route)


def contract_rows(left, right):
    return lax.dot_general(
        left, right, (((0,), (0,)), ((), ())), preferred_element_type=jnp.float32
    )


def contract_cols(left, right):
    return lax.dot_general(
        left, right, (((1,), (1,)), ((), ())), preferred_element_type=jnp.float32
    )


def exchange(block, groups):
    lead = block.shape[0]
    parted = block.reshape((groups, lead // groups) + block.shape[1:])
    moved = lax.all_to_all(parted, "expert", split_axis=0, concat_axis=0, tiled=True)
    return moved.reshape(block.shape)


def side_block(values):
    lanes = jnp.arange(128, dtype=jnp.int32)[None, :]
    return jnp.where(lanes == 0, values[:, None], jnp.zeros((), values.dtype))


def per_device(hidden_in, out_grad, routes, mixing, w_gate, w_up, w_down):
    tokens_in = hidden_in[0]
    grads_in = out_grad[0]
    groups = lax.axis_size("expert")
    tok_rows = tokens_in.shape[0]
    model_width = tokens_in.shape[1]
    capacity = 4 * tok_rows // groups
    slot_total = groups * capacity
    gate_mat = w_gate[0, 0]
    up_mat = w_up[0, 0]
    down_mat = w_down[0, 0]

    chosen = routes[0].reshape(-1)
    onehot = (chosen[:, None] == jnp.arange(groups, dtype=jnp.int32)[None, :]).astype(jnp.int32)
    slot_rank = jnp.sum(onehot * (jnp.cumsum(onehot, axis=0) - 1), axis=1)
    slot_index = (chosen * capacity + slot_rank).reshape(tok_rows, 2)
    slot_ids = jnp.arange(slot_total, dtype=jnp.int32)
    hit = slot_index[None, :, :] == slot_ids[:, None, None]
    pick = jnp.any(hit, axis=2).astype(jnp.bfloat16)

    send_rows = jnp.dot(pick, tokens_in, preferred_element_type=jnp.float32).astype(jnp.bfloat16)
    send_grads = jnp.dot(pick, grads_in, preferred_element_type=jnp.float32).astype(jnp.bfloat16)
    slot_weight = jnp.sum(
        jnp.where(hit, mixing[0][None, :, :].astype(jnp.float32), 0.0), axis=(1, 2)
    ).astype(jnp.bfloat16)
    send_grads = jnp.concatenate([send_grads, side_block(slot_weight)], axis=1)

    rows_in = exchange(send_rows, groups)
    grad_ext = exchange(send_grads, groups)
    grad_rows = grad_ext[:, :model_width]
    weight_in = grad_ext[:, model_width]

    pre_gate = jnp.dot(rows_in, gate_mat, preferred_element_type=jnp.float32)
    pre_up = jnp.dot(rows_in, up_mat, preferred_element_type=jnp.float32)
    sigmoid_g = jax.nn.sigmoid(pre_gate)
    silu_g = pre_gate * sigmoid_g
    act_rows = (silu_g * pre_up).astype(jnp.bfloat16)
    expert_out = jnp.dot(act_rows, down_mat, preferred_element_type=jnp.float32).astype(
        jnp.bfloat16
    )
    prob_part = jnp.sum(
        grad_rows.astype(jnp.float32) * expert_out.astype(jnp.float32), axis=1
    ).astype(jnp.bfloat16)
    scaled = (weight_in.astype(jnp.float32)[:, None] * grad_rows.astype(jnp.float32)).astype(
        jnp.bfloat16
    )
    act_grad = contract_cols(scaled, down_mat)
    gate_pre = (act_grad * pre_up * sigmoid_g * (1.0 + pre_gate * (1.0 - sigmoid_g))).astype(
        jnp.bfloat16
    )
    up_pre = (act_grad * silu_g).astype(jnp.bfloat16)
    in_grad = (contract_cols(gate_pre, gate_mat) + contract_cols(up_pre, up_mat)).astype(
        jnp.bfloat16
    )

    back_ext = exchange(jnp.concatenate([in_grad, side_block(prob_part)], axis=1), groups)
    back_grad = back_ext[:, :model_width]
    back_prob = back_ext[:, model_width]

    grad_down = contract_rows(act_rows, scaled).astype(jnp.bfloat16)
    grad_gate = contract_rows(rows_in, gate_pre).astype(jnp.bfloat16)
    grad_up = contract_rows(rows_in, up_pre).astype(jnp.bfloat16)

    input_grad = (
        grads_in.astype(jnp.float32) + contract_rows(pick, back_grad)
    ).astype(jnp.bfloat16)
    prob_grad = jnp.sum(
        jnp.where(hit, back_prob.astype(jnp.float32)[:, None, None], 0.0), axis=0
    ).astype(jnp.bfloat16)
    handed = shifted(input_grad, "section", -1)
    return (
        grad_gate[None, None],
        grad_up[None, None],
        grad_down[None, None],
        handed[None],
        prob_grad[None],
    )


def solution(mesh):
    placed = (
        P("section", "expert", None),
        P("section", "expert", None),
        P("section", "expert", None),
        P("section", "expert", None),
        P("section", "expert", None, None),
        P("section", "expert", None, None),
        P("section", "expert", None, None),
    )
    return jax.shard_map(
        per_device,
        mesh=mesh,
        in_specs=placed,
        out_specs=(
            P("section", "expert", None, None),
            P("section", "expert", None, None),
            P("section", "expert", None, None),
            P("section", "expert", None),
            P("section", "expert", None),
        ),
        check_vma=False,
    )
```

```python
import jax
import jax.numpy as jnp
from jax import lax
from jax.sharding import PartitionSpec as P


def shifted(block, axis, distance):
    devices = range(lax.axis_size(axis))
    route = [(i - distance, i) for i in devices if i - distance in devices]
    return lax.ppermute(block, axis, route)


def contract_rows(left, right):
    return lax.dot_general(
        left, right, (((0,), (0,)), ((), ())), preferred_element_type=jnp.float32
    )


def contract_cols(left, right):
    return lax.dot_general(
        left, right, (((1,), (1,)), ((), ())), preferred_element_type=jnp.float32
    )


def exchange(block, groups):
    lead = block.shape[0]
    parted = block.reshape((groups, lead // groups) + block.shape[1:])
    moved = lax.all_to_all(parted, "expert", split_axis=0, concat_axis=0, tiled=True)
    return moved.reshape(block.shape)


def side_block(values):
    lanes = jnp.arange(128, dtype=jnp.int32)[None, :]
    return jnp.where(lanes == 0, values[:, None], jnp.zeros((), values.dtype))


def expert_chunk(rows_in, grad_ext, gate_mat, up_mat, down_mat, model_width):
    grad_rows = grad_ext[:, :model_width]
    weight_in = grad_ext[:, model_width]
    pre_gate = jnp.dot(rows_in, gate_mat, preferred_element_type=jnp.float32)
    pre_up = jnp.dot(rows_in, up_mat, preferred_element_type=jnp.float32)
    sigmoid_g = jax.nn.sigmoid(pre_gate)
    silu_g = pre_gate * sigmoid_g
    act_rows = (silu_g * pre_up).astype(jnp.bfloat16)
    expert_out = jnp.dot(act_rows, down_mat, preferred_element_type=jnp.float32).astype(
        jnp.bfloat16
    )
    prob_part = jnp.sum(
        grad_rows.astype(jnp.float32) * expert_out.astype(jnp.float32), axis=1
    ).astype(jnp.bfloat16)
    scaled = (weight_in.astype(jnp.float32)[:, None] * grad_rows.astype(jnp.float32)).astype(
        jnp.bfloat16
    )
    act_grad = contract_cols(scaled, down_mat)
    gate_pre = (act_grad * pre_up * sigmoid_g * (1.0 + pre_gate * (1.0 - sigmoid_g))).astype(
        jnp.bfloat16
    )
    up_pre = (act_grad * silu_g).astype(jnp.bfloat16)
    in_grad = (contract_cols(gate_pre, gate_mat) + contract_cols(up_pre, up_mat)).astype(
        jnp.bfloat16
    )
    back_ext = jnp.concatenate([in_grad, side_block(prob_part)], axis=1)
    return back_ext, act_rows, scaled, gate_pre, up_pre


def per_device(hidden_in, out_grad, routes, mixing, w_gate, w_up, w_down):
    tokens_in = hidden_in[0]
    grads_in = out_grad[0]
    groups = lax.axis_size("expert")
    tok_rows = tokens_in.shape[0]
    model_width = tokens_in.shape[1]
    capacity = 4 * tok_rows // groups
    slot_total = groups * capacity
    chunks = 2 if capacity % 2 == 0 else 1
    sub = capacity // chunks
    gate_mat = w_gate[0, 0]
    up_mat = w_up[0, 0]
    down_mat = w_down[0, 0]

    chosen = routes[0].reshape(-1)
    onehot = (chosen[:, None] == jnp.arange(groups, dtype=jnp.int32)[None, :]).astype(jnp.int32)
    slot_rank = jnp.sum(onehot * (jnp.cumsum(onehot, axis=0) - 1), axis=1)
    slot_index = (chosen * capacity + slot_rank).reshape(tok_rows, 2)
    slot_ids = jnp.arange(slot_total, dtype=jnp.int32)
    hit = slot_index[None, :, :] == slot_ids[:, None, None]
    pick = jnp.any(hit, axis=2).astype(jnp.bfloat16).reshape(groups, capacity, tok_rows)
    slot_weight = jnp.sum(
        jnp.where(hit, mixing[0][None, :, :].astype(jnp.float32), 0.0), axis=(1, 2)
    ).astype(jnp.bfloat16).reshape(groups, capacity)

    picks, backs, saved = [], [], []
    for c in range(chunks):
        pick_c = pick[:, c * sub:(c + 1) * sub, :].reshape(groups * sub, tok_rows)
        weight_c = slot_weight[:, c * sub:(c + 1) * sub].reshape(groups * sub)
        send_rows = jnp.dot(pick_c, tokens_in, preferred_element_type=jnp.float32).astype(
            jnp.bfloat16
        )
        send_grads = jnp.dot(pick_c, grads_in, preferred_element_type=jnp.float32).astype(
            jnp.bfloat16
        )
        send_grads = jnp.concatenate([send_grads, side_block(weight_c)], axis=1)
        rows_in = exchange(send_rows, groups)
        grad_ext = exchange(send_grads, groups)
        back_ext, act_rows, scaled, gate_pre, up_pre = expert_chunk(
            rows_in, grad_ext, gate_mat, up_mat, down_mat, model_width
        )
        picks.append(pick_c)
        backs.append(exchange(back_ext, groups))
        saved.append((rows_in, act_rows, scaled, gate_pre, up_pre))

    grad_down = sum(contract_rows(a, s) for _, a, s, _, _ in saved).astype(jnp.bfloat16)
    grad_gate = sum(contract_rows(r, g) for r, _, _, g, _ in saved).astype(jnp.bfloat16)
    grad_up = sum(contract_rows(r, u) for r, _, _, _, u in saved).astype(jnp.bfloat16)

    combined = sum(contract_rows(p, b[:, :model_width]) for p, b in zip(picks, backs))
    input_grad = (grads_in.astype(jnp.float32) + combined).astype(jnp.bfloat16)
    back_prob = jnp.concatenate(
        [b[:, model_width].reshape(groups, sub) for b in backs], axis=1
    ).reshape(slot_total)
    prob_grad = jnp.sum(
        jnp.where(hit, back_prob.astype(jnp.float32)[:, None, None], 0.0), axis=0
    ).astype(jnp.bfloat16)
    handed = shifted(input_grad, "section", -1)
    return (
        grad_gate[None, None],
        grad_up[None, None],
        grad_down[None, None],
        handed[None],
        prob_grad[None],
    )


def solution(mesh):
    placed = (
        P("section", "expert", None),
        P("section", "expert", None),
        P("section", "expert", None),
        P("section", "expert", None),
        P("section", "expert", None, None),
        P("section", "expert", None, None),
        P("section", "expert", None, None),
    )
    return jax.shard_map(
        per_device,
        mesh=mesh,
        in_specs=placed,
        out_specs=(
            P("section", "expert", None, None),
            P("section", "expert", None, None),
            P("section", "expert", None, None),
            P("section", "expert", None),
            P("section", "expert", None),
        ),
        check_vma=False,
    )
```

```python
import jax
import jax.numpy as jnp
from jax import lax
from jax.sharding import PartitionSpec as P


def shifted(block, axis, distance):
    devices = range(lax.axis_size(axis))
    route = [(i - distance, i) for i in devices if i - distance in devices]
    return lax.ppermute(block, axis, route)


def contract_rows(left, right):
    return lax.dot_general(
        left, right, (((0,), (0,)), ((), ())), preferred_element_type=jnp.float32
    )


def contract_cols(left, right):
    return lax.dot_general(
        left, right, (((1,), (1,)), ((), ())), preferred_element_type=jnp.float32
    )


def exchange(block, groups):
    lead = block.shape[0]
    parted = block.reshape((groups, lead // groups) + block.shape[1:])
    moved = lax.all_to_all(parted, "expert", split_axis=0, concat_axis=0, tiled=True)
    return moved.reshape(block.shape)


def side_block(values):
    lanes = jnp.arange(128, dtype=jnp.int32)[None, :]
    return jnp.where(lanes == 0, values[:, None], jnp.zeros((), values.dtype))


def per_device(hidden_in, out_grad, routes, mixing, w_gate, w_up, w_down):
    tokens_in = hidden_in[0]
    grads_in = out_grad[0]
    groups = lax.axis_size("expert")
    tok_rows = tokens_in.shape[0]
    model_width = tokens_in.shape[1]
    capacity = 4 * tok_rows // groups
    slot_total = groups * capacity
    gate_mat = w_gate[0, 0]
    up_mat = w_up[0, 0]
    down_mat = w_down[0, 0]

    chosen = routes[0].reshape(-1)
    onehot = (chosen[:, None] == jnp.arange(groups, dtype=jnp.int32)[None, :]).astype(jnp.int32)
    slot_rank = jnp.sum(onehot * (jnp.cumsum(onehot, axis=0) - 1), axis=1)
    slot_index = (chosen * capacity + slot_rank).reshape(tok_rows, 2)
    slot_ids = jnp.arange(slot_total, dtype=jnp.int32)
    hit = slot_index[None, :, :] == slot_ids[:, None, None]
    pick = jnp.any(hit, axis=2).astype(jnp.bfloat16)

    send_rows = jnp.dot(pick, tokens_in, preferred_element_type=jnp.float32).astype(jnp.bfloat16)
    send_grads = jnp.dot(pick, grads_in, preferred_element_type=jnp.float32).astype(jnp.bfloat16)
    slot_weight = jnp.sum(
        jnp.where(hit, mixing[0][None, :, :].astype(jnp.float32), 0.0), axis=(1, 2)
    ).astype(jnp.bfloat16)
    send_grads = jnp.concatenate([send_grads, side_block(slot_weight)], axis=1)

    rows_in = exchange(send_rows, groups)
    grad_ext = exchange(send_grads, groups)
    grad_rows = grad_ext[:, :model_width]
    weight_in = grad_ext[:, model_width]

    pre_gate = jnp.dot(rows_in, gate_mat, preferred_element_type=jnp.float32)
    pre_up = jnp.dot(rows_in, up_mat, preferred_element_type=jnp.float32)
    sigmoid_g = jax.nn.sigmoid(pre_gate)
    silu_g = pre_gate * sigmoid_g
    act_rows = (silu_g * pre_up).astype(jnp.bfloat16)
    expert_out = jnp.dot(act_rows, down_mat, preferred_element_type=jnp.float32).astype(
        jnp.bfloat16
    )
    pre_gate, pre_up, act_rows, expert_out = lax.optimization_barrier(
        (pre_gate, pre_up, act_rows, expert_out)
    )
    sigmoid_g = jax.nn.sigmoid(pre_gate)
    silu_g = pre_gate * sigmoid_g
    prob_part = jnp.sum(
        grad_rows.astype(jnp.float32) * expert_out.astype(jnp.float32), axis=1
    ).astype(jnp.bfloat16)
    scaled = (weight_in.astype(jnp.float32)[:, None] * grad_rows.astype(jnp.float32)).astype(
        jnp.bfloat16
    )
    act_grad = contract_cols(scaled, down_mat)
    gate_pre = (act_grad * pre_up * sigmoid_g * (1.0 + pre_gate * (1.0 - sigmoid_g))).astype(
        jnp.bfloat16
    )
    up_pre = (act_grad * silu_g).astype(jnp.bfloat16)
    in_grad = (contract_cols(gate_pre, gate_mat) + contract_cols(up_pre, up_mat)).astype(
        jnp.bfloat16
    )

    back_ext = exchange(jnp.concatenate([in_grad, side_block(prob_part)], axis=1), groups)
    back_grad = back_ext[:, :model_width]
    back_prob = back_ext[:, model_width]

    grad_down = contract_rows(act_rows, scaled).astype(jnp.bfloat16)
    grad_gate = contract_rows(rows_in, gate_pre).astype(jnp.bfloat16)
    grad_up = contract_rows(rows_in, up_pre).astype(jnp.bfloat16)

    input_grad = (
        grads_in.astype(jnp.float32) + contract_rows(pick, back_grad)
    ).astype(jnp.bfloat16)
    prob_grad = jnp.sum(
        jnp.where(hit, back_prob.astype(jnp.float32)[:, None, None], 0.0), axis=0
    ).astype(jnp.bfloat16)
    handed = shifted(input_grad, "section", -1)
    return (
        grad_gate[None, None],
        grad_up[None, None],
        grad_down[None, None],
        handed[None],
        prob_grad[None],
    )


def solution(mesh):
    placed = (
        P("section", "expert", None),
        P("section", "expert", None),
        P("section", "expert", None),
        P("section", "expert", None),
        P("section", "expert", None, None),
        P("section", "expert", None, None),
        P("section", "expert", None, None),
    )
    return jax.shard_map(
        per_device,
        mesh=mesh,
        in_specs=placed,
        out_specs=(
            P("section", "expert", None, None),
            P("section", "expert", None, None),
            P("section", "expert", None, None),
            P("section", "expert", None),
            P("section", "expert", None),
        ),
        check_vma=False,
    )
```

```python
import jax
import jax.numpy as jnp
from jax import lax
from jax.sharding import PartitionSpec as P


def shifted(block, axis, distance):
    devices = range(lax.axis_size(axis))
    route = [(i - distance, i) for i in devices if i - distance in devices]
    return lax.ppermute(block, axis, route)


def contract_rows(left, right):
    return lax.dot_general(
        left, right, (((0,), (0,)), ((), ())), preferred_element_type=jnp.float32
    )


def contract_cols(left, right):
    return lax.dot_general(
        left, right, (((1,), (1,)), ((), ())), preferred_element_type=jnp.float32
    )


def exchange(block, groups):
    lead = block.shape[0]
    parted = block.reshape((groups, lead // groups) + block.shape[1:])
    moved = lax.all_to_all(parted, "expert", split_axis=0, concat_axis=0, tiled=True)
    return moved.reshape(block.shape)


def lane_block(values, width, lane):
    lanes = jnp.arange(width, dtype=jnp.int32)[None, :]
    return jnp.where(lanes == lane, values.astype(jnp.float32)[:, None], 0.0)


def per_device(hidden_in, out_grad, routes, mixing, w_gate, w_up, w_down):
    tokens_in = hidden_in[0]
    grads_in = out_grad[0]
    groups = lax.axis_size("expert")
    tok_rows = tokens_in.shape[0]
    model_width = tokens_in.shape[1]
    side = 128
    capacity = 4 * tok_rows // groups
    slot_total = groups * capacity
    gate_mat = w_gate[0, 0]
    up_mat = w_up[0, 0]
    down_mat = w_down[0, 0]
    hidden_units = gate_mat.shape[1]

    chosen = routes[0].reshape(-1)
    onehot = (chosen[:, None] == jnp.arange(groups, dtype=jnp.int32)[None, :]).astype(jnp.int32)
    slot_rank = jnp.sum(onehot * (jnp.cumsum(onehot, axis=0) - 1), axis=1)
    slot_index = (chosen * capacity + slot_rank).reshape(tok_rows, 2)
    slot_ids = jnp.arange(slot_total, dtype=jnp.int32)
    hit = slot_index[None, :, :] == slot_ids[:, None, None]
    pick = jnp.any(hit, axis=2).astype(jnp.bfloat16)
    slot_weight = jnp.sum(
        jnp.where(hit, mixing[0][None, :, :].astype(jnp.float32), 0.0), axis=(1, 2)
    ).astype(jnp.bfloat16)

    both = jnp.concatenate(
        [tokens_in, grads_in, jnp.zeros((tok_rows, side), jnp.bfloat16)], axis=1
    )
    send_width = 2 * model_width + side
    send = (
        jnp.dot(pick, both, preferred_element_type=jnp.float32)
        + lane_block(slot_weight, send_width, 2 * model_width)
    ).astype(jnp.bfloat16)
    recv = exchange(send, groups)
    rows_in = recv[:, :model_width]
    grad_rows = recv[:, model_width:2 * model_width]
    weight_in = recv[:, 2 * model_width]

    pre_gate = jnp.dot(rows_in, gate_mat, preferred_element_type=jnp.float32)
    pre_up = jnp.dot(rows_in, up_mat, preferred_element_type=jnp.float32)
    sigmoid_g = jax.nn.sigmoid(pre_gate)
    silu_g = pre_gate * sigmoid_g
    act_rows = (silu_g * pre_up).astype(jnp.bfloat16)
    expert_out = jnp.dot(act_rows, down_mat, preferred_element_type=jnp.float32).astype(
        jnp.bfloat16
    )
    prob_part = jnp.sum(
        grad_rows.astype(jnp.float32) * expert_out.astype(jnp.float32), axis=1
    ).astype(jnp.bfloat16)
    scaled = (weight_in.astype(jnp.float32)[:, None] * grad_rows.astype(jnp.float32)).astype(
        jnp.bfloat16
    )
    act_grad = contract_cols(scaled, down_mat)
    gate_pre = (act_grad * pre_up * sigmoid_g * (1.0 + pre_gate * (1.0 - sigmoid_g))).astype(
        jnp.bfloat16
    )
    up_pre = (act_grad * silu_g).astype(jnp.bfloat16)
    pad_rows = jnp.zeros((side, hidden_units), jnp.bfloat16)
    gate_ext = jnp.concatenate([gate_mat, pad_rows], axis=0)
    up_ext = jnp.concatenate([up_mat, pad_rows], axis=0)
    back_width = model_width + side
    in_grad_ext = (
        (contract_cols(gate_pre, gate_ext) + contract_cols(up_pre, up_ext))
        + lane_block(prob_part, back_width, model_width)
    ).astype(jnp.bfloat16)

    back_ext = exchange(in_grad_ext, groups)
    back_grad = back_ext[:, :model_width]
    back_prob = back_ext[:, model_width]

    grad_down = contract_rows(act_rows, scaled).astype(jnp.bfloat16)
    grad_gate = contract_rows(rows_in, gate_pre).astype(jnp.bfloat16)
    grad_up = contract_rows(rows_in, up_pre).astype(jnp.bfloat16)

    input_grad = (
        grads_in.astype(jnp.float32) + contract_rows(pick, back_grad)
    ).astype(jnp.bfloat16)
    prob_grad = jnp.sum(
        jnp.where(hit, back_prob.astype(jnp.float32)[:, None, None], 0.0), axis=0
    ).astype(jnp.bfloat16)
    handed = shifted(input_grad, "section", -1)
    return (
        grad_gate[None, None],
        grad_up[None, None],
        grad_down[None, None],
        handed[None],
        prob_grad[None],
    )


def solution(mesh):
    placed = (
        P("section", "expert", None),
        P("section", "expert", None),
        P("section", "expert", None),
        P("section", "expert", None),
        P("section", "expert", None, None),
        P("section", "expert", None, None),
        P("section", "expert", None, None),
    )
    return jax.shard_map(
        per_device,
        mesh=mesh,
        in_specs=placed,
        out_specs=(
            P("section", "expert", None, None),
            P("section", "expert", None, None),
            P("section", "expert", None, None),
            P("section", "expert", None),
            P("section", "expert", None),
        ),
        check_vma=False,
    )
```

```python
import jax
import jax.numpy as jnp
from jax import lax
from jax.sharding import PartitionSpec as P


def shifted(block, axis, distance):
    devices = range(lax.axis_size(axis))
    route = [(i - distance, i) for i in devices if i - distance in devices]
    return lax.ppermute(block, axis, route)


def contract_rows(left, right):
    return lax.dot_general(
        left, right, (((0,), (0,)), ((), ())), preferred_element_type=jnp.float32
    )


def contract_cols(left, right):
    return lax.dot_general(
        left, right, (((1,), (1,)), ((), ())), preferred_element_type=jnp.float32
    )


def exchange(block, groups):
    lead = block.shape[0]
    parted = block.reshape((groups, lead // groups) + block.shape[1:])
    moved = lax.all_to_all(parted, "expert", split_axis=0, concat_axis=0, tiled=True)
    return moved.reshape(block.shape)


def side_block(values):
    lanes = jnp.arange(128, dtype=jnp.int32)[None, :]
    return jnp.where(lanes == 0, values[:, None], jnp.zeros((), values.dtype))


def per_device(hidden_in, out_grad, routes, mixing, w_gate, w_up, w_down):
    tokens_in = hidden_in[0]
    grads_in = out_grad[0]
    groups = lax.axis_size("expert")
    tok_rows = tokens_in.shape[0]
    model_width = tokens_in.shape[1]
    capacity = 4 * tok_rows // groups
    slot_total = groups * capacity
    gate_mat = w_gate[0, 0]
    up_mat = w_up[0, 0]
    down_mat = w_down[0, 0]

    chosen = routes[0].reshape(-1)
    onehot = (chosen[:, None] == jnp.arange(groups, dtype=jnp.int32)[None, :]).astype(jnp.int32)
    slot_rank = jnp.sum(onehot * (jnp.cumsum(onehot, axis=0) - 1), axis=1)
    slot_index = (chosen * capacity + slot_rank).reshape(tok_rows, 2)
    slot_ids = jnp.arange(slot_total, dtype=jnp.int32)
    hit = slot_index[None, :, :] == slot_ids[:, None, None]
    pick = jnp.any(hit, axis=2).astype(jnp.bfloat16)

    send_rows = jnp.dot(pick, tokens_in, preferred_element_type=jnp.float32).astype(jnp.bfloat16)
    send_grads = jnp.dot(pick, grads_in, preferred_element_type=jnp.float32).astype(jnp.bfloat16)
    slot_weight = jnp.sum(
        jnp.where(hit, mixing[0][None, :, :].astype(jnp.float32), 0.0), axis=(1, 2)
    ).astype(jnp.bfloat16)
    send_grads = jnp.concatenate([send_grads, side_block(slot_weight)], axis=1)

    rows_in = exchange(send_rows, groups)
    grad_ext = exchange(send_grads, groups)
    grad_rows = grad_ext[:, :model_width]
    weight_in = grad_ext[:, model_width]

    pre_gate = jnp.dot(rows_in, gate_mat, preferred_element_type=jnp.float32)
    pre_up = jnp.dot(rows_in, up_mat, preferred_element_type=jnp.float32)
    sigmoid_g = jax.nn.sigmoid(pre_gate)
    silu_g = pre_gate * sigmoid_g
    act_rows = (silu_g * pre_up).astype(jnp.bfloat16)
    expert_out = jnp.dot(act_rows, down_mat, preferred_element_type=jnp.float32).astype(
        jnp.bfloat16
    )
    pre_gate, pre_up, act_rows, expert_out = lax.optimization_barrier(
        (pre_gate, pre_up, act_rows, expert_out)
    )
    sigmoid_g = jax.nn.sigmoid(pre_gate)
    silu_g = pre_gate * sigmoid_g
    prob_part = jnp.sum(
        grad_rows.astype(jnp.float32) * expert_out.astype(jnp.float32), axis=1
    ).astype(jnp.bfloat16)
    scaled = (weight_in.astype(jnp.float32)[:, None] * grad_rows.astype(jnp.float32)).astype(
        jnp.bfloat16
    )
    act_grad = contract_cols(scaled, down_mat)
    gate_pre = (act_grad * pre_up * sigmoid_g * (1.0 + pre_gate * (1.0 - sigmoid_g))).astype(
        jnp.bfloat16
    )
    up_pre = (act_grad * silu_g).astype(jnp.bfloat16)
    in_grad = (contract_cols(gate_pre, gate_mat) + contract_cols(up_pre, up_mat)).astype(
        jnp.bfloat16
    )

    back_grad = exchange(in_grad, groups)
    back_prob = exchange(prob_part, groups)

    grad_down = contract_rows(act_rows, scaled).astype(jnp.bfloat16)
    grad_gate = contract_rows(rows_in, gate_pre).astype(jnp.bfloat16)
    grad_up = contract_rows(rows_in, up_pre).astype(jnp.bfloat16)

    input_grad = (
        grads_in.astype(jnp.float32) + contract_rows(pick, back_grad)
    ).astype(jnp.bfloat16)
    prob_grad = jnp.sum(
        jnp.where(hit, back_prob.astype(jnp.float32)[:, None, None], 0.0), axis=0
    ).astype(jnp.bfloat16)
    handed = shifted(input_grad, "section", -1)
    return (
        grad_gate[None, None],
        grad_up[None, None],
        grad_down[None, None],
        handed[None],
        prob_grad[None],
    )


def solution(mesh):
    placed = (
        P("section", "expert", None),
        P("section", "expert", None),
        P("section", "expert", None),
        P("section", "expert", None),
        P("section", "expert", None, None),
        P("section", "expert", None, None),
        P("section", "expert", None, None),
    )
    return jax.shard_map(
        per_device,
        mesh=mesh,
        in_specs=placed,
        out_specs=(
            P("section", "expert", None, None),
            P("section", "expert", None, None),
            P("section", "expert", None, None),
            P("section", "expert", None),
            P("section", "expert", None),
        ),
        check_vma=False,
    )
```

```python
import jax
import jax.numpy as jnp
from jax import lax
from jax.sharding import PartitionSpec as P


def shifted(block, axis, distance):
    devices = range(lax.axis_size(axis))
    route = [(i - distance, i) for i in devices if i - distance in devices]
    return lax.ppermute(block, axis, route)


def contract_rows(left, right):
    return lax.dot_general(
        left, right, (((0,), (0,)), ((), ())), preferred_element_type=jnp.float32
    )


def contract_cols(left, right):
    return lax.dot_general(
        left, right, (((1,), (1,)), ((), ())), preferred_element_type=jnp.float32
    )


def exchange(block, groups):
    lead = block.shape[0]
    parted = block.reshape((groups, lead // groups) + block.shape[1:])
    moved = lax.all_to_all(parted, "expert", split_axis=0, concat_axis=0, tiled=True)
    return moved.reshape(block.shape)


def side_block(values):
    lanes = jnp.arange(128, dtype=jnp.int32)[None, :]
    return jnp.where(lanes == 0, values[:, None], jnp.zeros((), values.dtype))


def device_body(hidden_in, out_grad, routes, mixing, w_gate, w_up, w_down):
    tokens_in = hidden_in[0]
    grads_in = out_grad[0]
    groups = lax.axis_size("expert")
    tok_rows = tokens_in.shape[0]
    model_width = tokens_in.shape[1]
    capacity = 4 * tok_rows // groups
    slot_total = groups * capacity
    gate_mat = w_gate[0, 0]
    up_mat = w_up[0, 0]
    down_mat = w_down[0, 0]

    chosen = routes[0].reshape(-1)
    onehot = (chosen[:, None] == jnp.arange(groups, dtype=jnp.int32)[None, :]).astype(jnp.int32)
    slot_rank = jnp.sum(onehot * (jnp.cumsum(onehot, axis=0) - 1), axis=1)
    slot_index = (chosen * capacity + slot_rank).reshape(tok_rows, 2)
    slot_ids = jnp.arange(slot_total, dtype=jnp.int32)
    hit = slot_index[None, :, :] == slot_ids[:, None, None]
    pick = jnp.any(hit, axis=2).astype(jnp.bfloat16)

    send_rows = jnp.dot(pick, tokens_in, preferred_element_type=jnp.float32).astype(jnp.bfloat16)
    send_grads = jnp.dot(pick, grads_in, preferred_element_type=jnp.float32).astype(jnp.bfloat16)
    slot_weight = jnp.sum(
        jnp.where(hit, mixing[0][None, :, :].astype(jnp.float32), 0.0), axis=(1, 2)
    ).astype(jnp.bfloat16)
    send_grads = jnp.concatenate([send_grads, side_block(slot_weight)], axis=1)

    rows_in = exchange(send_rows, groups)
    grad_ext = exchange(send_grads, groups)
    grad_rows = grad_ext[:, :model_width]
    weight_in = grad_ext[:, model_width]

    pre_gate = jnp.dot(rows_in, gate_mat, preferred_element_type=jnp.float32)
    pre_up = jnp.dot(rows_in, up_mat, preferred_element_type=jnp.float32)
    sigmoid_g = jax.nn.sigmoid(pre_gate)
    silu_g = pre_gate * sigmoid_g
    act_rows = (silu_g * pre_up).astype(jnp.bfloat16)
    expert_out = jnp.dot(act_rows, down_mat, preferred_element_type=jnp.float32).astype(
        jnp.bfloat16
    )
    pre_gate, pre_up, act_rows, expert_out = lax.optimization_barrier(
        (pre_gate, pre_up, act_rows, expert_out)
    )
    sigmoid_g = jax.nn.sigmoid(pre_gate)
    silu_g = pre_gate * sigmoid_g
    prob_part = jnp.sum(
        grad_rows.astype(jnp.float32) * expert_out.astype(jnp.float32), axis=1
    ).astype(jnp.bfloat16)
    scaled = (weight_in.astype(jnp.float32)[:, None] * grad_rows.astype(jnp.float32)).astype(
        jnp.bfloat16
    )
    act_grad = contract_cols(scaled, down_mat)
    gate_pre = (act_grad * pre_up * sigmoid_g * (1.0 + pre_gate * (1.0 - sigmoid_g))).astype(
        jnp.bfloat16
    )
    up_pre = (act_grad * silu_g).astype(jnp.bfloat16)
    in_grad = (contract_cols(gate_pre, gate_mat) + contract_cols(up_pre, up_mat)).astype(
        jnp.bfloat16
    )

    back_grad = exchange(in_grad, groups)
    back_prob = exchange(prob_part, groups)

    grad_down = contract_rows(act_rows, scaled).astype(jnp.bfloat16)
    grad_gate = contract_rows(rows_in, gate_pre).astype(jnp.bfloat16)
    grad_up = contract_rows(rows_in, up_pre).astype(jnp.bfloat16)

    half = tok_rows // 2 if tok_rows % 16 == 0 else tok_rows
    handed_parts = []
    for lo in range(0, tok_rows, half):
        part = (
            grads_in[lo:lo + half].astype(jnp.float32)
            + contract_rows(pick[:, lo:lo + half], back_grad)
        ).astype(jnp.bfloat16)
        handed_parts.append(shifted(part, "section", -1))
    handed = jnp.concatenate(handed_parts, axis=0)
    prob_grad = jnp.sum(
        jnp.where(hit, back_prob.astype(jnp.float32)[:, None, None], 0.0), axis=0
    ).astype(jnp.bfloat16)
    return (
        grad_gate[None, None],
        grad_up[None, None],
        grad_down[None, None],
        handed[None],
        prob_grad[None],
    )


def solution(mesh):
    placed = (
        P("section", "expert", None),
        P("section", "expert", None),
        P("section", "expert", None),
        P("section", "expert", None),
        P("section", "expert", None, None),
        P("section", "expert", None, None),
        P("section", "expert", None, None),
    )
    return jax.shard_map(
        device_body,
        mesh=mesh,
        in_specs=placed,
        out_specs=(
            P("section", "expert", None, None),
            P("section", "expert", None, None),
            P("section", "expert", None, None),
            P("section", "expert", None),
            P("section", "expert", None),
        ),
        check_vma=False,
    )
```

```python
import jax
import jax.numpy as jnp
from jax import lax
from jax.sharding import PartitionSpec as P


def shifted(block, axis, distance):
    devices = range(lax.axis_size(axis))
    route = [(i - distance, i) for i in devices if i - distance in devices]
    return lax.ppermute(block, axis, route)


def contract_rows(left, right):
    return lax.dot_general(
        left, right, (((0,), (0,)), ((), ())), preferred_element_type=jnp.float32
    )


def contract_cols(left, right):
    return lax.dot_general(
        left, right, (((1,), (1,)), ((), ())), preferred_element_type=jnp.float32
    )


def exchange(block, groups):
    lead = block.shape[0]
    parted = block.reshape((groups, lead // groups) + block.shape[1:])
    moved = lax.all_to_all(parted, "expert", split_axis=0, concat_axis=0, tiled=True)
    return moved.reshape(block.shape)


def side_block(values):
    lanes = jnp.arange(128, dtype=jnp.int32)[None, :]
    return jnp.where(lanes == 0, values[:, None], jnp.zeros((), values.dtype))


def device_body(hidden_in, out_grad, routes, mixing, w_gate, w_up, w_down):
    tokens_in = hidden_in[0]
    grads_in = out_grad[0]
    groups = lax.axis_size("expert")
    tok_rows = tokens_in.shape[0]
    model_width = tokens_in.shape[1]
    capacity = 4 * tok_rows // groups
    slot_total = groups * capacity
    gate_mat = w_gate[0, 0]
    up_mat = w_up[0, 0]
    down_mat = w_down[0, 0]

    chosen = routes[0].reshape(-1)
    onehot = (chosen[:, None] == jnp.arange(groups, dtype=jnp.int32)[None, :]).astype(jnp.int32)
    slot_rank = jnp.sum(onehot * (jnp.cumsum(onehot, axis=0) - 1), axis=1)
    slot_index = (chosen * capacity + slot_rank).reshape(tok_rows, 2)
    slot_ids = jnp.arange(slot_total, dtype=jnp.int32)
    hit = slot_index[None, :, :] == slot_ids[:, None, None]
    pick = jnp.any(hit, axis=2).astype(jnp.bfloat16)

    send_rows = jnp.dot(pick, tokens_in, preferred_element_type=jnp.float32).astype(jnp.bfloat16)
    send_grads = jnp.dot(pick, grads_in, preferred_element_type=jnp.float32).astype(jnp.bfloat16)
    slot_weight = jnp.sum(
        jnp.where(hit, mixing[0][None, :, :].astype(jnp.float32), 0.0), axis=(1, 2)
    ).astype(jnp.bfloat16)
    send_grads = jnp.concatenate([send_grads, side_block(slot_weight)], axis=1)

    rows_in = exchange(send_rows, groups)
    grad_ext = exchange(send_grads, groups)
    grad_rows = grad_ext[:, :model_width]
    weight_in = grad_ext[:, model_width]

    pre_gate = jnp.dot(rows_in, gate_mat, preferred_element_type=jnp.float32)
    pre_up = jnp.dot(rows_in, up_mat, preferred_element_type=jnp.float32)
    sigmoid_g = jax.nn.sigmoid(pre_gate)
    silu_g = pre_gate * sigmoid_g
    act_rows = (silu_g * pre_up).astype(jnp.bfloat16)
    expert_out = jnp.dot(act_rows, down_mat, preferred_element_type=jnp.float32).astype(
        jnp.bfloat16
    )
    pre_gate, pre_up, act_rows, expert_out = lax.optimization_barrier(
        (pre_gate, pre_up, act_rows, expert_out)
    )
    sigmoid_g = jax.nn.sigmoid(pre_gate)
    silu_g = pre_gate * sigmoid_g
    prob_part = jnp.sum(
        grad_rows.astype(jnp.float32) * expert_out.astype(jnp.float32), axis=1
    ).astype(jnp.bfloat16)
    scaled = (weight_in.astype(jnp.float32)[:, None] * grad_rows.astype(jnp.float32)).astype(
        jnp.bfloat16
    )
    act_grad = contract_cols(scaled, down_mat)
    gate_pre = (act_grad * pre_up * sigmoid_g * (1.0 + pre_gate * (1.0 - sigmoid_g))).astype(
        jnp.bfloat16
    )
    up_pre = (act_grad * silu_g).astype(jnp.bfloat16)
    in_grad = contract_cols(
        jnp.concatenate([gate_pre, up_pre], axis=1), jnp.concatenate([gate_mat, up_mat], axis=1)
    ).astype(jnp.bfloat16)

    back_grad = exchange(in_grad, groups)
    back_prob = exchange(prob_part, groups)

    grad_down = contract_rows(act_rows, scaled).astype(jnp.bfloat16)
    grad_gate = contract_rows(rows_in, gate_pre).astype(jnp.bfloat16)
    grad_up = contract_rows(rows_in, up_pre).astype(jnp.bfloat16)

    input_grad = (
        grads_in.astype(jnp.float32) + contract_rows(pick, back_grad)
    ).astype(jnp.bfloat16)
    prob_grad = jnp.sum(
        jnp.where(hit, back_prob.astype(jnp.float32)[:, None, None], 0.0), axis=0
    ).astype(jnp.bfloat16)
    handed = shifted(input_grad, "section", -1)
    return (
        grad_gate[None, None],
        grad_up[None, None],
        grad_down[None, None],
        handed[None],
        prob_grad[None],
    )


def solution(mesh):
    placed = (
        P("section", "expert", None),
        P("section", "expert", None),
        P("section", "expert", None),
        P("section", "expert", None),
        P("section", "expert", None, None),
        P("section", "expert", None, None),
        P("section", "expert", None, None),
    )
    return jax.shard_map(
        device_body,
        mesh=mesh,
        in_specs=placed,
        out_specs=(
            P("section", "expert", None, None),
            P("section", "expert", None, None),
            P("section", "expert", None, None),
            P("section", "expert", None),
            P("section", "expert", None),
        ),
        check_vma=False,
    )
```

```python
import jax
import jax.numpy as jnp
from jax import lax
from jax.sharding import PartitionSpec as P


def shifted(block, axis, distance):
    devices = range(lax.axis_size(axis))
    route = [(i - distance, i) for i in devices if i - distance in devices]
    return lax.ppermute(block, axis, route)


def contract_rows(left, right):
    return lax.dot_general(
        left, right, (((0,), (0,)), ((), ())), preferred_element_type=jnp.float32
    )


def contract_cols(left, right):
    return lax.dot_general(
        left, right, (((1,), (1,)), ((), ())), preferred_element_type=jnp.float32
    )


def exchange(block, groups):
    lead = block.shape[0]
    parted = block.reshape((groups, lead // groups) + block.shape[1:])
    moved = lax.all_to_all(parted, "expert", split_axis=0, concat_axis=0, tiled=True)
    return moved.reshape(block.shape)


def side_block(values):
    lanes = jnp.arange(128, dtype=jnp.int32)[None, :]
    return jnp.where(lanes == 0, values[:, None], jnp.zeros((), values.dtype))


def device_body(hidden_in, out_grad, routes, mixing, w_gate, w_up, w_down):
    tokens_in = hidden_in[0]
    grads_in = out_grad[0]
    groups = lax.axis_size("expert")
    tok_rows = tokens_in.shape[0]
    model_width = tokens_in.shape[1]
    capacity = 4 * tok_rows // groups
    slot_total = groups * capacity
    gate_mat = w_gate[0, 0]
    up_mat = w_up[0, 0]
    down_mat = w_down[0, 0]

    chosen = routes[0].reshape(-1)
    onehot = (chosen[:, None] == jnp.arange(groups, dtype=jnp.int32)[None, :]).astype(jnp.int32)
    slot_rank = jnp.sum(onehot * (jnp.cumsum(onehot, axis=0) - 1), axis=1)
    slot_index = (chosen * capacity + slot_rank).reshape(tok_rows, 2)
    slot_ids = jnp.arange(slot_total, dtype=jnp.int32)
    hit = slot_index[None, :, :] == slot_ids[:, None, None]
    pick = jnp.any(hit, axis=2).astype(jnp.bfloat16)

    send_rows = jnp.dot(pick, tokens_in, preferred_element_type=jnp.float32).astype(jnp.bfloat16)
    send_grads = jnp.dot(pick, grads_in, preferred_element_type=jnp.float32).astype(jnp.bfloat16)
    slot_weight = jnp.sum(
        jnp.where(hit, mixing[0][None, :, :].astype(jnp.float32), 0.0), axis=(1, 2)
    ).astype(jnp.bfloat16)
    send_grads = jnp.concatenate([send_grads, side_block(slot_weight)], axis=1)

    rows_in = exchange(send_rows, groups)
    grad_ext = exchange(send_grads, groups)
    grad_rows = grad_ext[:, :model_width]
    weight_in = grad_ext[:, model_width]

    pre_gate = jnp.dot(rows_in, gate_mat, preferred_element_type=jnp.float32)
    pre_up = jnp.dot(rows_in, up_mat, preferred_element_type=jnp.float32)
    sigmoid_g = jax.nn.sigmoid(pre_gate)
    silu_g = pre_gate * sigmoid_g
    act_rows = (silu_g * pre_up).astype(jnp.bfloat16)
    expert_out = jnp.dot(act_rows, down_mat, preferred_element_type=jnp.float32).astype(
        jnp.bfloat16
    )
    pre_gate, pre_up, sigmoid_g, act_rows, expert_out = lax.optimization_barrier(
        (pre_gate, pre_up, sigmoid_g, act_rows, expert_out)
    )
    silu_g = pre_gate * sigmoid_g
    prob_part = jnp.sum(
        grad_rows.astype(jnp.float32) * expert_out.astype(jnp.float32), axis=1
    ).astype(jnp.bfloat16)
    scaled = (weight_in.astype(jnp.float32)[:, None] * grad_rows.astype(jnp.float32)).astype(
        jnp.bfloat16
    )
    act_grad = contract_cols(scaled, down_mat)
    gate_pre = (act_grad * pre_up * sigmoid_g * (1.0 + pre_gate * (1.0 - sigmoid_g))).astype(
        jnp.bfloat16
    )
    up_pre = (act_grad * silu_g).astype(jnp.bfloat16)
    in_grad = (contract_cols(gate_pre, gate_mat) + contract_cols(up_pre, up_mat)).astype(
        jnp.bfloat16
    )

    back_grad = exchange(in_grad, groups)
    back_prob = exchange(prob_part, groups)

    grad_down = contract_rows(act_rows, scaled).astype(jnp.bfloat16)
    grad_gate = contract_rows(rows_in, gate_pre).astype(jnp.bfloat16)
    grad_up = contract_rows(rows_in, up_pre).astype(jnp.bfloat16)

    input_grad = (
        grads_in.astype(jnp.float32) + contract_rows(pick, back_grad)
    ).astype(jnp.bfloat16)
    prob_grad = jnp.sum(
        jnp.where(hit, back_prob.astype(jnp.float32)[:, None, None], 0.0), axis=0
    ).astype(jnp.bfloat16)
    handed = shifted(input_grad, "section", -1)
    return (
        grad_gate[None, None],
        grad_up[None, None],
        grad_down[None, None],
        handed[None],
        prob_grad[None],
    )


def solution(mesh):
    placed = (
        P("section", "expert", None),
        P("section", "expert", None),
        P("section", "expert", None),
        P("section", "expert", None),
        P("section", "expert", None, None),
        P("section", "expert", None, None),
        P("section", "expert", None, None),
    )
    return jax.shard_map(
        device_body,
        mesh=mesh,
        in_specs=placed,
        out_specs=(
            P("section", "expert", None, None),
            P("section", "expert", None, None),
            P("section", "expert", None, None),
            P("section", "expert", None),
            P("section", "expert", None),
        ),
        check_vma=False,
    )
```
